1024 devices in a mesh: row: 16 (over z_lo, x), col: 64 (over z_hi, y, core).
Axes of the slice: x: 8, y: 8, z: 8 (z_hi: 4, z_lo: 2; z = z_hi * 2 + z_lo), core: 2. Of those that a mesh axis runs over, the one named last changes fastest.
Arguments:
- features: bfloat16 [131072, 512], P(('row', 'col')), may hold values from -6 to 6
- adj_tiles: bfloat16 [16, 512, 128, 128], P('row', 'col'), may hold values from -0.1875 to 0.1875
- tile_rows: int32 [16, 512], P('row', 'col'), may hold values from 0 to 63, as said below
- tile_cols: int32 [16, 512], P('row', 'col'), may hold values from 0 to 15
- tile_count: int32 [16, 64], P('row', 'col'), may hold values from 1 to 8, as said below
- weight: bfloat16 [1024, 512], replicated, may hold values from -0.25 to 0.25
- cotangent: bfloat16 [131072, 512], P(('row', 'col')), may hold values from -6 to 6
Outputs:
- hidden: bfloat16 [131072, 512], P(('row', 'col'))
- weight_grad: float32 [1024, 512], replicated
The draws below stay inside these ranges and needn't reach their ends.
Inputs may be any that keep to these rules, and one draw needn't show every extreme that they name: `tile_count`: some device has all 8 slots live. `tile_rows`: every slot of device (r, c) names tile row (c + k) mod 64 with 0 <= k < 4; slot 0 of every device has k = 3.
All inputs are finite; a program needn't handle non-finite values.
Results may differ from the reference program's by a relative error of at most 0.0035.
Values may be sent and summed in bfloat16 or wider, within the bound.
No kernel may reach another device: no remote copies, remote signals or barrier semaphores. Data moves between devices by JAX's collectives and lax.ppermute only.
A program may use at most 32 MiB of HBM per device.

```python
import jax
import jax.numpy as jnp
from jax import lax

F = 512
TILE = 128
REACH = 4
TPD = 8
NPD = 128
NODES = 131072
RB = 64
CB = 16
N_ROW = 16
N_COL = 64


def draw_tile_count(key, part):
    counts = jax.random.randint(key, (N_ROW * N_COL,), 1, TPD + 1)
    chosen = jax.random.randint(jax.random.fold_in(key, 7), (), 0, N_ROW * N_COL)
    counts = jnp.where(jnp.arange(N_ROW * N_COL) == chosen, TPD, counts)
    return counts.reshape(N_ROW, N_COL).astype(jnp.int32)


def draw_tile_rows(key, part):
    slots = jnp.arange(N_COL * TPD, dtype=jnp.int32)
    owner = slots // TPD
    offsets = jax.random.randint(key, (N_ROW, N_COL * TPD), 0, REACH)
    offsets = jnp.where((slots % TPD == 0)[None, :], REACH - 1, offsets)
    return ((owner[None, :] + offsets) % N_COL).astype(jnp.int32)


def with_ends(values, own_key, low, top_value):
    index_at = [jax.random.randint(jax.random.fold_in(own_key, axis), (), 0, length) for axis, length in enumerate(values.shape)]
    widest = values.shape.index(max(values.shape))
    next_to = index_at[:widest] + [(index_at[widest] + 1) % values.shape[widest]] + index_at[widest + 1:]
    return values.at[tuple(index_at)].set(low).at[tuple(next_to)].set(top_value)


def shard_levels(rng, dims, pieces, least, top_value):
    def one(axis_at, blocks):
        draws = jax.random.uniform(jax.random.fold_in(jax.random.fold_in(rng, 6), axis_at), (blocks,), jnp.float32, least / len(pieces), top_value / len(pieces))
        return jnp.repeat(jnp.exp(draws), dims[axis_at] // blocks).reshape((-1,) + (1,) * (len(dims) - axis_at - 1))

    factor_of = one(*pieces[0])
    for cut in pieces[1:]:
        factor_of = factor_of * one(*cut)
    return factor_of


def noise(own_key, dims, scale, limit, cuts=(), kind=jnp.bfloat16):
    loudness = shard_levels(own_key, dims, cuts, -0.22, 0.18) if cuts else 1.0
    entries = jax.random.normal(own_key, dims, jnp.float32) * scale * loudness
    return jnp.minimum(jnp.maximum(entries, -limit), limit).astype(kind)


def setup_inputs(seed: int = 0) -> dict:
    seeds = jax.random.split(jax.random.key(seed), 8)
    return {
        "features": noise(seeds[0], (NODES, F), 1.0, 6.0, ((0, 1024),)),
        "adj_tiles": noise(seeds[1], (N_ROW, N_COL * TPD, TILE, TILE), (TPD * TILE * TILE // NPD) ** -0.5, 0.1875, ((0, 16), (1, 64))),
        "tile_rows": draw_tile_rows(jax.random.fold_in(seeds[7], 71), 0),
        "tile_cols": with_ends(jax.random.randint(seeds[3], (N_ROW, N_COL * TPD), 0, CB), jax.random.fold_in(seeds[3], 1), 0, CB - 1).astype(jnp.int32),
        "tile_count": draw_tile_count(jax.random.fold_in(seeds[7], 71), 0),
        "weight": noise(seeds[5], (2 * F, F), F ** -0.5, 0.25),
        "cotangent": noise(seeds[6], (NODES, F), 1.0, 6.0, ((0, 1024),)),
    }


def tile_forward(adj_tiles, rows_idx, cols_idx, count, source, num_rows):
    width = source.shape[1]
    blocks = source.reshape(-1, TILE, width)
    chosen = jnp.take(blocks, cols_idx, axis=0).astype(jnp.float32)
    products = jnp.einsum('tij,tjx->tix', adj_tiles.astype(jnp.float32), chosen, precision=lax.Precision.HIGHEST)
    live_mask = (jnp.arange(adj_tiles.shape[0]) < count).astype(jnp.float32)
    placing = (rows_idx[:, None] == jnp.arange(num_rows)[None, :]).astype(jnp.float32) * live_mask[:, None]
    total = jnp.einsum('tr,tix->rix', placing, products, precision=lax.Precision.HIGHEST)
    return total.reshape(num_rows * TILE, width)


def tile_backward(adj_tiles, rows_idx, cols_idx, count, source, num_cols):
    width = source.shape[1]
    blocks = source.reshape(-1, TILE, width)
    chosen = jnp.take(blocks, rows_idx, axis=0).astype(jnp.float32)
    products = jnp.einsum('tji,tjx->tix', adj_tiles.astype(jnp.float32), chosen, precision=lax.Precision.HIGHEST)
    live_mask = (jnp.arange(adj_tiles.shape[0]) < count).astype(jnp.float32)
    placing = (cols_idx[:, None] == jnp.arange(num_cols)[None, :]).astype(jnp.float32) * live_mask[:, None]
    total = jnp.einsum('tc,tix->cix', placing, products, precision=lax.Precision.HIGHEST)
    return total.reshape(num_cols * TILE, width)


def reference(features, adj_tiles, tile_rows, tile_cols, tile_count, weight, cotangent):
    width = features.shape[1]
    total_nodes = features.shape[0]
    w_self = weight[:width]
    w_neigh = weight[width:]
    projected = jnp.dot(features, w_neigh, preferred_element_type=jnp.float32).astype(jnp.bfloat16)
    col_proj = projected.reshape(N_ROW, N_COL, NPD, width).transpose(1, 0, 2, 3).reshape(N_COL, N_ROW * NPD, width)
    col_feats = features.reshape(N_ROW, N_COL, NPD, width).transpose(1, 0, 2, 3).reshape(N_COL, N_ROW * NPD, width)
    grid_tiles = adj_tiles.reshape(N_ROW, N_COL, TPD, TILE, TILE)
    grid_rows = tile_rows.reshape(N_ROW, N_COL, TPD)
    grid_cols = tile_cols.reshape(N_ROW, N_COL, TPD)

    def row_slab(row_idx):
        def step(total, col_idx):
            part = tile_forward(grid_tiles[row_idx, col_idx], grid_rows[row_idx, col_idx], grid_cols[row_idx, col_idx],
                                tile_count[row_idx, col_idx], col_proj[col_idx], RB)
            return total + part, None
        total, _ = lax.scan(step, jnp.zeros((RB * TILE, width), jnp.float32), jnp.arange(N_COL, dtype=jnp.int32))
        return total

    neighbour = lax.map(row_slab, jnp.arange(N_ROW, dtype=jnp.int32)).reshape(total_nodes, width)
    pre_act = jnp.dot(features, w_self, preferred_element_type=jnp.float32) + neighbour
    hidden = jax.nn.silu(pre_act).astype(jnp.bfloat16)
    sigmoid_z = jax.nn.sigmoid(pre_act)
    slope = sigmoid_z * (1.0 + pre_act * (1.0 - sigmoid_z))
    upstream = (cotangent.astype(jnp.float32) * slope).astype(jnp.bfloat16)
    grad_self = jnp.dot(features.T, upstream, preferred_element_type=jnp.float32)
    row_up = upstream.reshape(N_ROW, N_COL * NPD, width)

    def back(total, device_idx):
        row_idx = device_idx // N_COL
        col_idx = device_idx % N_COL
        spread = tile_backward(grid_tiles[row_idx, col_idx], grid_rows[row_idx, col_idx], grid_cols[row_idx, col_idx],
                               tile_count[row_idx, col_idx], row_up[row_idx], CB)
        term = jnp.dot(col_feats[col_idx].astype(jnp.float32).T, spread, precision=lax.Precision.HIGHEST)
        return total + term, None

    grad_neigh, _ = lax.scan(back, jnp.zeros((width, width), jnp.float32), jnp.arange(N_ROW * N_COL, dtype=jnp.int32))
    weight_grad = jnp.concatenate([grad_self, grad_neigh], axis=0) * (float(total_nodes) ** -0.5)
    return hidden, weight_grad
```

```python
import jax
import jax.numpy as jnp
from jax import lax
from jax.sharding import Mesh, PartitionSpec as P

REACH = 4
ROW = ("zlo", "x")
COL = ("zhi", "y", "core")
ALL = ROW + COL


def from_behind(value, steps):
    count = lax.axis_size(COL)
    pairs = [(source, (source + steps) % count) for source in range(count)]
    return lax.ppermute(value, COL, pairs)


def reduce_all(stacked):
    part = stacked
    for axis in ("core", "y", "x"):
        part = lax.psum_scatter(part, axis, scatter_dimension=0, tiled=True)
    part = lax.psum(part, ("zhi", "zlo"))
    for axis in ("x", "y", "core"):
        part = lax.all_gather(part, axis, axis=0, tiled=True)
    return part


def gather_row(features):
    return lax.all_gather(features, ROW, axis=0, tiled=True)


def body(features, adj_tiles, tile_rows, tile_cols, tile_count, weight, cotangent):
    width = features.shape[1]
    own_nodes = features.shape[0]
    tile_size = adj_tiles.shape[2]
    row_count = lax.axis_size(ROW)
    col_count = lax.axis_size(COL)
    tiles = adj_tiles[0]
    slots = tiles.shape[0]
    cols = tile_cols[0]
    live = jnp.arange(slots) < tile_count[0, 0]
    offsets = (tile_rows[0] - lax.axis_index(COL)) % col_count
    w_self = weight[:width]
    w_neigh = weight[width:]

    col_feats = gather_row(features)
    chosen = jnp.take(col_feats.reshape(row_count, tile_size, width), cols, axis=0)
    projected = jnp.dot(chosen.reshape(slots * tile_size, width), w_neigh,
                        preferred_element_type=jnp.float32).astype(jnp.bfloat16)
    placing = (offsets[None, :] == jnp.arange(REACH)[:, None]) & live[None, :]
    placed = jnp.where(placing[:, :, None, None], tiles[None], jnp.zeros_like(tiles[None]))
    placed = placed.transpose(0, 2, 1, 3).reshape(REACH * tile_size, slots * tile_size)
    stacked_sums = jnp.dot(placed, projected, preferred_element_type=jnp.float32)
    stacked_sums = stacked_sums.reshape(REACH, tile_size, width)
    neighbour = stacked_sums[0]
    for step in range(1, REACH):
        neighbour = neighbour + from_behind(stacked_sums[step], step)

    pre_act = jnp.dot(features, w_self, preferred_element_type=jnp.float32) + neighbour
    hidden = jax.nn.silu(pre_act).astype(jnp.bfloat16)
    sigmoid_z = jax.nn.sigmoid(pre_act)
    slope = sigmoid_z * (1.0 + pre_act * (1.0 - sigmoid_z))
    upstream = (cotangent.astype(jnp.float32) * slope).astype(jnp.bfloat16)
    grad_self = jnp.dot(features.T, upstream, preferred_element_type=jnp.float32)

    window = [upstream] + [from_behind(upstream, -step) for step in range(1, REACH)]
    window = jnp.stack(window)
    reached = jnp.take(window, offsets, axis=0).reshape(slots * tile_size, width)
    mixed = jnp.einsum("tij,tjx->tix", tiles, chosen, preferred_element_type=jnp.float32)
    mixed = jnp.where(live[:, None, None], mixed, 0.0).reshape(slots * tile_size, width)
    high = mixed.astype(jnp.bfloat16)
    low = (mixed - high.astype(jnp.float32)).astype(jnp.bfloat16)
    grad_neigh = jnp.dot(high.T, reached, preferred_element_type=jnp.float32)
    grad_neigh = grad_neigh + jnp.dot(low.T, reached, preferred_element_type=jnp.float32)

    stacked = jnp.concatenate([grad_self, grad_neigh], axis=0)
    summed = reduce_all(stacked)
    total_nodes = own_nodes * row_count * col_count
    weight_grad = summed * float(total_nodes) ** (-0.5)
    return (hidden, weight_grad)


def solution(mesh):
    rows, cols = mesh.devices.shape
    fine = Mesh(mesh.devices.reshape(2, rows // 2, 4, cols // 8, 2), ALL)
    in_specs = (
        P(ALL, None),
        P(ROW, COL, None, None),
        P(ROW, COL),
        P(ROW, COL),
        P(ROW, COL),
        P(),
        P(ALL, None),
    )
    out_specs = (P(ALL, None), P())
    return jax.shard_map(body, mesh=fine, in_specs=in_specs, out_specs=out_specs, check_vma=False)
```

```python
import jax
import jax.numpy as jnp
from jax import lax
from jax.sharding import Mesh, PartitionSpec as P

REACH = 4
ROW = ("zlo", "x")
COL = ("zhi", "y", "core")
ALL = ROW + COL


def from_behind(value, steps):
    count = lax.axis_size(COL)
    pairs = [(source, (source + steps) % count) for source in range(count)]
    return lax.ppermute(value, COL, pairs)


def exchange_sum(part, axes):
    peers = lax.axis_size(axes)
    pieces = part.reshape(peers, part.shape[0] // peers, part.shape[1])
    pieces = lax.all_to_all(pieces, axes, 0, 0, tiled=True)
    return pieces.sum(axis=0)


def exchange_gather(part, axes):
    peers = lax.axis_size(axes)
    copies = jnp.broadcast_to(part[None], (peers,) + part.shape)
    copies = lax.all_to_all(copies, axes, 0, 0, tiled=True)
    return copies.reshape(peers * part.shape[0], *part.shape[1:])


def reduce_all(stacked):
    part = exchange_sum(stacked, COL)
    part = exchange_sum(part, ROW)
    part = exchange_gather(part, ROW)
    return exchange_gather(part, COL)


def gather_row(features):
    return exchange_gather(features, ROW)


def body(features, adj_tiles, tile_rows, tile_cols, tile_count, weight, cotangent):
    width = features.shape[1]
    own_nodes = features.shape[0]
    tile_size = adj_tiles.shape[2]
    row_count = lax.axis_size(ROW)
    col_count = lax.axis_size(COL)
    tiles = adj_tiles[0]
    slots = tiles.shape[0]
    cols = tile_cols[0]
    live = jnp.arange(slots) < tile_count[0, 0]
    offsets = (tile_rows[0] - lax.axis_index(COL)) % col_count
    w_self = weight[:width]
    w_neigh = weight[width:]

    col_feats = gather_row(features)
    chosen = jnp.take(col_feats.reshape(row_count, tile_size, width), cols, axis=0)
    projected = jnp.dot(chosen.reshape(slots * tile_size, width), w_neigh,
                        preferred_element_type=jnp.float32).astype(jnp.bfloat16)
    placing = (offsets[None, :] == jnp.arange(REACH)[:, None]) & live[None, :]
    placed = jnp.where(placing[:, :, None, None], tiles[None], jnp.zeros_like(tiles[None]))
    placed = placed.transpose(0, 2, 1, 3).reshape(REACH * tile_size, slots * tile_size)
    stacked_sums = jnp.dot(placed, projected, preferred_element_type=jnp.float32)
    stacked_sums = stacked_sums.reshape(REACH, tile_size, width)
    neighbour = stacked_sums[0]
    for step in range(1, REACH):
        neighbour = neighbour + from_behind(stacked_sums[step], step)

    pre_act = jnp.dot(features, w_self, preferred_element_type=jnp.float32) + neighbour
    hidden = jax.nn.silu(pre_act).astype(jnp.bfloat16)
    sigmoid_z = jax.nn.sigmoid(pre_act)
    slope = sigmoid_z * (1.0 + pre_act * (1.0 - sigmoid_z))
    upstream = (cotangent.astype(jnp.float32) * slope).astype(jnp.bfloat16)
    grad_self = jnp.dot(features.T, upstream, preferred_element_type=jnp.float32)

    window = [upstream] + [from_behind(upstream, -step) for step in range(1, REACH)]
    window = jnp.stack(window)
    reached = jnp.take(window, offsets, axis=0).reshape(slots * tile_size, width)
    mixed = jnp.einsum("tij,tjx->tix", tiles, chosen, preferred_element_type=jnp.float32)
    mixed = jnp.where(live[:, None, None], mixed, 0.0).reshape(slots * tile_size, width)
    high = mixed.astype(jnp.bfloat16)
    low = (mixed - high.astype(jnp.float32)).astype(jnp.bfloat16)
    grad_neigh = jnp.dot(high.T, reached, preferred_element_type=jnp.float32)
    grad_neigh = grad_neigh + jnp.dot(low.T, reached, preferred_element_type=jnp.float32)

    stacked = jnp.concatenate([grad_self, grad_neigh], axis=0)
    summed = reduce_all(stacked)
    total_nodes = own_nodes * row_count * col_count
    weight_grad = summed * float(total_nodes) ** (-0.5)
    return (hidden, weight_grad)


def solution(mesh):
    rows, cols = mesh.devices.shape
    fine = Mesh(mesh.devices.reshape(2, rows // 2, 4, cols // 8, 2), ALL)
    in_specs = (
        P(ALL, None),
        P(ROW, COL, None, None),
        P(ROW, COL),
        P(ROW, COL),
        P(ROW, COL),
        P(),
        P(ALL, None),
    )
    out_specs = (P(ALL, None), P())
    return jax.shard_map(body, mesh=fine, in_specs=in_specs, out_specs=out_specs, check_vma=False)
```

```python
import jax
import jax.numpy as jnp
from jax import lax
from jax.sharding import Mesh, PartitionSpec as P

REACH = 4
ROW = ("zlo", "x")
COL = ("zhi", "y", "core")
ALL = ROW + COL


def from_behind(value, steps):
    count = lax.axis_size(COL)
    pairs = [(source, (source + steps) % count) for source in range(count)]
    return lax.ppermute(value, COL, pairs)


def exchange_sum(part, axes):
    peers = lax.axis_size(axes)
    pieces = part.reshape(peers, part.shape[0] // peers, part.shape[1])
    pieces = lax.all_to_all(pieces, axes, 0, 0, tiled=True)
    return pieces.sum(axis=0)


def exchange_gather(part, axes):
    peers = lax.axis_size(axes)
    copies = jnp.broadcast_to(part[None], (peers,) + part.shape)
    copies = lax.all_to_all(copies, axes, 0, 0, tiled=True)
    return copies.reshape(peers * part.shape[0], *part.shape[1:])


def reduce_all(stacked):
    part = exchange_sum(stacked, "core")
    part = exchange_sum(part, ("zhi", "y"))
    part = exchange_sum(part, ROW)
    part = exchange_gather(part, ROW)
    part = exchange_gather(part, ("zhi", "y"))
    return exchange_gather(part, "core")


def gather_row(features):
    return exchange_gather(features, ROW)


def body(features, adj_tiles, tile_rows, tile_cols, tile_count, weight, cotangent):
    width = features.shape[1]
    own_nodes = features.shape[0]
    tile_size = adj_tiles.shape[2]
    row_count = lax.axis_size(ROW)
    col_count = lax.axis_size(COL)
    tiles = adj_tiles[0]
    slots = tiles.shape[0]
    cols = tile_cols[0]
    live = jnp.arange(slots) < tile_count[0, 0]
    offsets = (tile_rows[0] - lax.axis_index(COL)) % col_count
    w_self = weight[:width]
    w_neigh = weight[width:]

    col_feats = gather_row(features)
    chosen = jnp.take(col_feats.reshape(row_count, tile_size, width), cols, axis=0)
    projected = jnp.dot(chosen.reshape(slots * tile_size, width), w_neigh,
                        preferred_element_type=jnp.float32).astype(jnp.bfloat16)
    placing = (offsets[None, :] == jnp.arange(REACH)[:, None]) & live[None, :]
    placed = jnp.where(placing[:, :, None, None], tiles[None], jnp.zeros_like(tiles[None]))
    placed = placed.transpose(0, 2, 1, 3).reshape(REACH * tile_size, slots * tile_size)
    stacked_sums = jnp.dot(placed, projected, preferred_element_type=jnp.float32)
    stacked_sums = stacked_sums.reshape(REACH, tile_size, width)
    neighbour = stacked_sums[0]
    for step in range(1, REACH):
        neighbour = neighbour + from_behind(stacked_sums[step], step)

    pre_act = jnp.dot(features, w_self, preferred_element_type=jnp.float32) + neighbour
    hidden = jax.nn.silu(pre_act).astype(jnp.bfloat16)
    sigmoid_z = jax.nn.sigmoid(pre_act)
    slope = sigmoid_z * (1.0 + pre_act * (1.0 - sigmoid_z))
    upstream = (cotangent.astype(jnp.float32) * slope).astype(jnp.bfloat16)
    grad_self = jnp.dot(features.T, upstream, preferred_element_type=jnp.float32)

    window = [upstream] + [from_behind(upstream, -step) for step in range(1, REACH)]
    window = jnp.stack(window)
    reached = jnp.take(window, offsets, axis=0).reshape(slots * tile_size, width)
    mixed = jnp.einsum("tij,tjx->tix", tiles, chosen, preferred_element_type=jnp.float32)
    mixed = jnp.where(live[:, None, None], mixed, 0.0).reshape(slots * tile_size, width)
    high = mixed.astype(jnp.bfloat16)
    low = (mixed - high.astype(jnp.float32)).astype(jnp.bfloat16)
    grad_neigh = jnp.dot(high.T, reached, preferred_element_type=jnp.float32)
    grad_neigh = grad_neigh + jnp.dot(low.T, reached, preferred_element_type=jnp.float32)

    stacked = jnp.concatenate([grad_self, grad_neigh], axis=0)
    summed = reduce_all(stacked)
    total_nodes = own_nodes * row_count * col_count
    weight_grad = summed * float(total_nodes) ** (-0.5)
    return (hidden, weight_grad)


def solution(mesh):
    rows, cols = mesh.devices.shape
    fine = Mesh(mesh.devices.reshape(2, rows // 2, 4, cols // 8, 2), ALL)
    in_specs = (
        P(ALL, None),
        P(ROW, COL, None, None),
        P(ROW, COL),
        P(ROW, COL),
        P(ROW, COL),
        P(),
        P(ALL, None),
    )
    out_specs = (P(ALL, None), P())
    return jax.shard_map(body, mesh=fine, in_specs=in_specs, out_specs=out_specs, check_vma=False)
```

```python
import jax
import jax.numpy as jnp
from jax import lax
from jax.sharding import Mesh, PartitionSpec as P

REACH = 4
ROW = ("zlo", "x")
COL = ("zhi", "y", "core")
ALL = ROW + COL


def from_behind(value, steps):
    count = lax.axis_size(COL)
    pairs = [(source, (source + steps) % count) for source in range(count)]
    return lax.ppermute(value, COL, pairs)


def exchange_sum(part, axes):
    peers = lax.axis_size(axes)
    pieces = part.reshape(peers, part.shape[0] // peers, part.shape[1])
    pieces = lax.all_to_all(pieces, axes, 0, 0, tiled=True)
    return pieces.sum(axis=0)


def exchange_gather(part, axes):
    peers = lax.axis_size(axes)
    copies = jnp.broadcast_to(part[None], (peers,) + part.shape)
    copies = lax.all_to_all(copies, axes, 0, 0, tiled=True)
    return copies.reshape(peers * part.shape[0], *part.shape[1:])


def reduce_all(stacked):
    part = exchange_sum(stacked, "core")
    part = exchange_sum(part, ROW)
    part = exchange_sum(part, ("zhi", "y"))
    part = exchange_gather(part, ("zhi", "y"))
    part = exchange_gather(part, ROW)
    return exchange_gather(part, "core")


def gather_row(features):
    return exchange_gather(features, ROW)


def body(features, adj_tiles, tile_rows, tile_cols, tile_count, weight, cotangent):
    width = features.shape[1]
    own_nodes = features.shape[0]
    tile_size = adj_tiles.shape[2]
    row_count = lax.axis_size(ROW)
    col_count = lax.axis_size(COL)
    tiles = adj_tiles[0]
    slots = tiles.shape[0]
    cols = tile_cols[0]
    live = jnp.arange(slots) < tile_count[0, 0]
    offsets = (tile_rows[0] - lax.axis_index(COL)) % col_count
    w_self = weight[:width]
    w_neigh = weight[width:]

    col_feats = gather_row(features)
    chosen = jnp.take(col_feats.reshape(row_count, tile_size, width), cols, axis=0)
    projected = jnp.dot(chosen.reshape(slots * tile_size, width), w_neigh,
                        preferred_element_type=jnp.float32).astype(jnp.bfloat16)
    placing = (offsets[None, :] == jnp.arange(REACH)[:, None]) & live[None, :]
    placed = jnp.where(placing[:, :, None, None], tiles[None], jnp.zeros_like(tiles[None]))
    placed = placed.transpose(0, 2, 1, 3).reshape(REACH * tile_size, slots * tile_size)
    stacked_sums = jnp.dot(placed, projected, preferred_element_type=jnp.float32)
    stacked_sums = stacked_sums.reshape(REACH, tile_size, width)
    neighbour = stacked_sums[0]
    for step in range(1, REACH):
        neighbour = neighbour + from_behind(stacked_sums[step], step)

    pre_act = jnp.dot(features, w_self, preferred_element_type=jnp.float32) + neighbour
    hidden = jax.nn.silu(pre_act).astype(jnp.bfloat16)
    sigmoid_z = jax.nn.sigmoid(pre_act)
    slope = sigmoid_z * (1.0 + pre_act * (1.0 - sigmoid_z))
    upstream = (cotangent.astype(jnp.float32) * slope).astype(jnp.bfloat16)
    grad_self = jnp.dot(features.T, upstream, preferred_element_type=jnp.float32)

    window = [upstream] + [from_behind(upstream, -step) for step in range(1, REACH)]
    window = jnp.stack(window)
    reached = jnp.take(window, offsets, axis=0).reshape(slots * tile_size, width)
    mixed = jnp.einsum("tij,tjx->tix", tiles, chosen, preferred_element_type=jnp.float32)
    mixed = jnp.where(live[:, None, None], mixed, 0.0).reshape(slots * tile_size, width)
    high = mixed.astype(jnp.bfloat16)
    low = (mixed - high.astype(jnp.float32)).astype(jnp.bfloat16)
    grad_neigh = jnp.dot(high.T, reached, preferred_element_type=jnp.float32)
    grad_neigh = grad_neigh + jnp.dot(low.T, reached, preferred_element_type=jnp.float32)

    stacked = jnp.concatenate([grad_self, grad_neigh], axis=0)
    summed = reduce_all(stacked)
    total_nodes = own_nodes * row_count * col_count
    weight_grad = summed * float(total_nodes) ** (-0.5)
    return (hidden, weight_grad)


def solution(mesh):
    rows, cols = mesh.devices.shape
    fine = Mesh(mesh.devices.reshape(2, rows // 2, 4, cols // 8, 2), ALL)
    in_specs = (
        P(ALL, None),
        P(ROW, COL, None, None),
        P(ROW, COL),
        P(ROW, COL),
        P(ROW, COL),
        P(),
        P(ALL, None),
    )
    out_specs = (P(ALL, None), P())
    return jax.shard_map(body, mesh=fine, in_specs=in_specs, out_specs=out_specs, check_vma=False)
```

```python
import jax
import jax.numpy as jnp
from jax import lax
from jax.sharding import Mesh, PartitionSpec as P

REACH = 4
ROW = ("zlo", "x")
COL = ("zhi", "y", "core")
ALL = ROW + COL


def from_behind(value, steps):
    count = lax.axis_size(COL)
    pairs = [(source, (source + steps) % count) for source in range(count)]
    return lax.ppermute(value, COL, pairs)


def exchange_sum(part, axes):
    peers = lax.axis_size(axes)
    pieces = part.reshape(peers, part.shape[0] // peers, part.shape[1])
    pieces = lax.all_to_all(pieces, axes, 0, 0, tiled=True)
    return pieces.sum(axis=0)


def exchange_gather(part, axes):
    peers = lax.axis_size(axes)
    copies = jnp.broadcast_to(part[None], (peers,) + part.shape)
    copies = lax.all_to_all(copies, axes, 0, 0, tiled=True)
    return copies.reshape(peers * part.shape[0], *part.shape[1:])


def reduce_all(stacked, scale):
    part = exchange_sum(stacked, "core")
    part = exchange_sum(part, ROW)
    part = exchange_sum(part, ("zhi", "y"))
    part = (part * scale).astype(jnp.bfloat16)
    part = exchange_gather(part, ("zhi", "y"))
    part = exchange_gather(part, ROW)
    return exchange_gather(part, "core").astype(jnp.float32)


def gather_row(features):
    return exchange_gather(features, ROW)


def body(features, adj_tiles, tile_rows, tile_cols, tile_count, weight, cotangent):
    width = features.shape[1]
    own_nodes = features.shape[0]
    tile_size = adj_tiles.shape[2]
    row_count = lax.axis_size(ROW)
    col_count = lax.axis_size(COL)
    tiles = adj_tiles[0]
    slots = tiles.shape[0]
    cols = tile_cols[0]
    live = jnp.arange(slots) < tile_count[0, 0]
    offsets = (tile_rows[0] - lax.axis_index(COL)) % col_count
    w_self = weight[:width]
    w_neigh = weight[width:]

    col_feats = gather_row(features)
    chosen = jnp.take(col_feats.reshape(row_count, tile_size, width), cols, axis=0)
    projected = jnp.dot(chosen.reshape(slots * tile_size, width), w_neigh,
                        preferred_element_type=jnp.float32).astype(jnp.bfloat16)
    placing = (offsets[None, :] == jnp.arange(REACH)[:, None]) & live[None, :]
    placed = jnp.where(placing[:, :, None, None], tiles[None], jnp.zeros_like(tiles[None]))
    placed = placed.transpose(0, 2, 1, 3).reshape(REACH * tile_size, slots * tile_size)
    stacked_sums = jnp.dot(placed, projected, preferred_element_type=jnp.float32)
    stacked_sums = stacked_sums.reshape(REACH, tile_size, width)
    neighbour = stacked_sums[0]
    for step in range(1, REACH):
        neighbour = neighbour + from_behind(stacked_sums[step], step)

    pre_act = jnp.dot(features, w_self, preferred_element_type=jnp.float32) + neighbour
    hidden = jax.nn.silu(pre_act).astype(jnp.bfloat16)
    sigmoid_z = jax.nn.sigmoid(pre_act)
    slope = sigmoid_z * (1.0 + pre_act * (1.0 - sigmoid_z))
    upstream = (cotangent.astype(jnp.float32) * slope).astype(jnp.bfloat16)
    grad_self = jnp.dot(features.T, upstream, preferred_element_type=jnp.float32)

    window = [upstream] + [from_behind(upstream, -step) for step in range(1, REACH)]
    window = jnp.stack(window)
    reached = jnp.take(window, offsets, axis=0).reshape(slots * tile_size, width)
    mixed = jnp.einsum("tij,tjx->tix", tiles, chosen, preferred_element_type=jnp.float32)
    mixed = jnp.where(live[:, None, None], mixed, 0.0).reshape(slots * tile_size, width)
    high = mixed.astype(jnp.bfloat16)
    low = (mixed - high.astype(jnp.float32)).astype(jnp.bfloat16)
    grad_neigh = jnp.dot(high.T, reached, preferred_element_type=jnp.float32)
    grad_neigh = grad_neigh + jnp.dot(low.T, reached, preferred_element_type=jnp.float32)

    stacked = jnp.concatenate([grad_self, grad_neigh], axis=0)
    total_nodes = own_nodes * row_count * col_count
    weight_grad = reduce_all(stacked, float(total_nodes) ** (-0.5))
    return (hidden, weight_grad)


def solution(mesh):
    rows, cols = mesh.devices.shape
    fine = Mesh(mesh.devices.reshape(2, rows // 2, 4, cols // 8, 2), ALL)
    in_specs = (
        P(ALL, None),
        P(ROW, COL, None, None),
        P(ROW, COL),
        P(ROW, COL),
        P(ROW, COL),
        P(),
        P(ALL, None),
    )
    out_specs = (P(ALL, None), P())
    return jax.shard_map(body, mesh=fine, in_specs=in_specs, out_specs=out_specs, check_vma=False)
```

```python
import jax
import jax.numpy as jnp
from jax import lax
from jax.sharding import Mesh, PartitionSpec as P

REACH = 4
ROW = ("zlo", "x")
COL = ("zhi", "y", "core")
ALL = ROW + COL


def from_behind(value, steps):
    count = lax.axis_size(COL)
    pairs = [(source, (source + steps) % count) for source in range(count)]
    return lax.ppermute(value, COL, pairs)


def exchange_sum(part, axes):
    peers = lax.axis_size(axes)
    pieces = part.reshape(peers, part.shape[0] // peers, part.shape[1])
    pieces = lax.all_to_all(pieces, axes, 0, 0, tiled=True)
    return pieces.sum(axis=0)


def exchange_gather(part, axes):
    peers = lax.axis_size(axes)
    copies = jnp.broadcast_to(part[None], (peers,) + part.shape)
    copies = lax.all_to_all(copies, axes, 0, 0, tiled=True)
    return copies.reshape(peers * part.shape[0], *part.shape[1:])


def reduce_all(stacked, scale):
    part = exchange_sum(stacked, "core")
    part = exchange_sum(part, ROW + ("zhi", "y"))
    part = (part * scale).astype(jnp.bfloat16)
    part = exchange_gather(part, ROW + ("zhi", "y"))
    return exchange_gather(part, "core").astype(jnp.float32)


def gather_row(features):
    return exchange_gather(features, ROW)


def body(features, adj_tiles, tile_rows, tile_cols, tile_count, weight, cotangent):
    width = features.shape[1]
    own_nodes = features.shape[0]
    tile_size = adj_tiles.shape[2]
    row_count = lax.axis_size(ROW)
    col_count = lax.axis_size(COL)
    tiles = adj_tiles[0]
    slots = tiles.shape[0]
    cols = tile_cols[0]
    live = jnp.arange(slots) < tile_count[0, 0]
    offsets = (tile_rows[0] - lax.axis_index(COL)) % col_count
    w_self = weight[:width]
    w_neigh = weight[width:]

    col_feats = gather_row(features)
    chosen = jnp.take(col_feats.reshape(row_count, tile_size, width), cols, axis=0)
    projected = jnp.dot(chosen.reshape(slots * tile_size, width), w_neigh,
                        preferred_element_type=jnp.float32).astype(jnp.bfloat16)
    placing = (offsets[None, :] == jnp.arange(REACH)[:, None]) & live[None, :]
    placed = jnp.where(placing[:, :, None, None], tiles[None], jnp.zeros_like(tiles[None]))
    placed = placed.transpose(0, 2, 1, 3).reshape(REACH * tile_size, slots * tile_size)
    stacked_sums = jnp.dot(placed, projected, preferred_element_type=jnp.float32)
    stacked_sums = stacked_sums.reshape(REACH, tile_size, width)
    neighbour = stacked_sums[0]
    for step in range(1, REACH):
        neighbour = neighbour + from_behind(stacked_sums[step], step)

    pre_act = jnp.dot(features, w_self, preferred_element_type=jnp.float32) + neighbour
    hidden = jax.nn.silu(pre_act).astype(jnp.bfloat16)
    sigmoid_z = jax.nn.sigmoid(pre_act)
    slope = sigmoid_z * (1.0 + pre_act * (1.0 - sigmoid_z))
    upstream = (cotangent.astype(jnp.float32) * slope).astype(jnp.bfloat16)
    grad_self = jnp.dot(features.T, upstream, preferred_element_type=jnp.float32)

    window = [upstream] + [from_behind(upstream, -step) for step in range(1, REACH)]
    window = jnp.stack(window)
    reached = jnp.take(window, offsets, axis=0).reshape(slots * tile_size, width)
    mixed = jnp.einsum("tij,tjx->tix", tiles, chosen, preferred_element_type=jnp.float32)
    mixed = jnp.where(live[:, None, None], mixed, 0.0).reshape(slots * tile_size, width)
    high = mixed.astype(jnp.bfloat16)
    low = (mixed - high.astype(jnp.float32)).astype(jnp.bfloat16)
    grad_neigh = jnp.dot(high.T, reached, preferred_element_type=jnp.float32)
    grad_neigh = grad_neigh + jnp.dot(low.T, reached, preferred_element_type=jnp.float32)

    stacked = jnp.concatenate([grad_self, grad_neigh], axis=0)
    total_nodes = own_nodes * row_count * col_count
    weight_grad = reduce_all(stacked, float(total_nodes) ** (-0.5))
    return (hidden, weight_grad)


def solution(mesh):
    rows, cols = mesh.devices.shape
    fine = Mesh(mesh.devices.reshape(2, rows // 2, 4, cols // 8, 2), ALL)
    in_specs = (
        P(ALL, None),
        P(ROW, COL, None, None),
        P(ROW, COL),
        P(ROW, COL),
        P(ROW, COL),
        P(),
        P(ALL, None),
    )
    out_specs = (P(ALL, None), P())
    return jax.shard_map(body, mesh=fine, in_specs=in_specs, out_specs=out_specs, check_vma=False)
```

```python
import jax
import jax.numpy as jnp
from jax import lax
from jax.sharding import Mesh, PartitionSpec as P

REACH = 4
ROW = ("zlo", "x")
COL = ("zhi", "y", "core")
ALL = ROW + COL


def from_behind(value, steps):
    count = lax.axis_size(COL)
    pairs = [(source, (source + steps) % count) for source in range(count)]
    return lax.ppermute(value, COL, pairs)


def exchange_sum(part, axes):
    peers = lax.axis_size(axes)
    pieces = part.reshape(peers, part.shape[0] // peers, part.shape[1])
    pieces = lax.all_to_all(pieces, axes, 0, 0, tiled=True)
    return pieces.sum(axis=0)


def exchange_gather(part, axes):
    peers = lax.axis_size(axes)
    copies = jnp.broadcast_to(part[None], (peers,) + part.shape)
    copies = lax.all_to_all(copies, axes, 0, 0, tiled=True)
    return copies.reshape(peers * part.shape[0], *part.shape[1:])


def reduce_all(stacked, scale):
    part = exchange_sum(stacked, "core")
    part = exchange_sum(part, ROW)
    part = exchange_sum(part, ("zhi", "y"))
    part = (part * scale).astype(jnp.bfloat16)
    part = exchange_gather(part, ("zhi", "y"))
    part = exchange_gather(part, ROW)
    return exchange_gather(part, "core").astype(jnp.float32)


def gather_row(features):
    part = exchange_gather(features, "x")
    return exchange_gather(part, "zlo")


def body(features, adj_tiles, tile_rows, tile_cols, tile_count, weight, cotangent):
    width = features.shape[1]
    own_nodes = features.shape[0]
    tile_size = adj_tiles.shape[2]
    row_count = lax.axis_size(ROW)
    col_count = lax.axis_size(COL)
    tiles = adj_tiles[0]
    slots = tiles.shape[0]
    cols = tile_cols[0]
    live = jnp.arange(slots) < tile_count[0, 0]
    offsets = (tile_rows[0] - lax.axis_index(COL)) % col_count
    w_self = weight[:width]
    w_neigh = weight[width:]

    col_feats = gather_row(features)
    chosen = jnp.take(col_feats.reshape(row_count, tile_size, width), cols, axis=0)
    projected = jnp.dot(chosen.reshape(slots * tile_size, width), w_neigh,
                        preferred_element_type=jnp.float32).astype(jnp.bfloat16)
    placing = (offsets[None, :] == jnp.arange(REACH)[:, None]) & live[None, :]
    placed = jnp.where(placing[:, :, None, None], tiles[None], jnp.zeros_like(tiles[None]))
    placed = placed.transpose(0, 2, 1, 3).reshape(REACH * tile_size, slots * tile_size)
    stacked_sums = jnp.dot(placed, projected, preferred_element_type=jnp.float32)
    stacked_sums = stacked_sums.reshape(REACH, tile_size, width)
    neighbour = stacked_sums[0]
    for step in range(1, REACH):
        neighbour = neighbour + from_behind(stacked_sums[step], step)

    pre_act = jnp.dot(features, w_self, preferred_element_type=jnp.float32) + neighbour
    hidden = jax.nn.silu(pre_act).astype(jnp.bfloat16)
    sigmoid_z = jax.nn.sigmoid(pre_act)
    slope = sigmoid_z * (1.0 + pre_act * (1.0 - sigmoid_z))
    upstream = (cotangent.astype(jnp.float32) * slope).astype(jnp.bfloat16)
    grad_self = jnp.dot(features.T, upstream, preferred_element_type=jnp.float32)

    window = [upstream] + [from_behind(upstream, -step) for step in range(1, REACH)]
    window = jnp.stack(window)
    reached = jnp.take(window, offsets, axis=0).reshape(slots * tile_size, width)
    mixed = jnp.einsum("tij,tjx->tix", tiles, chosen, preferred_element_type=jnp.float32)
    mixed = jnp.where(live[:, None, None], mixed, 0.0).reshape(slots * tile_size, width)
    high = mixed.astype(jnp.bfloat16)
    low = (mixed - high.astype(jnp.float32)).astype(jnp.bfloat16)
    grad_neigh = jnp.dot(high.T, reached, preferred_element_type=jnp.float32)
    grad_neigh = grad_neigh + jnp.dot(low.T, reached, preferred_element_type=jnp.float32)

    stacked = jnp.concatenate([grad_self, grad_neigh], axis=0)
    total_nodes = own_nodes * row_count * col_count
    weight_grad = reduce_all(stacked, float(total_nodes) ** (-0.5))
    return (hidden, weight_grad)


def solution(mesh):
    rows, cols = mesh.devices.shape
    fine = Mesh(mesh.devices.reshape(2, rows // 2, 4, cols // 8, 2), ALL)
    in_specs = (
        P(ALL, None),
        P(ROW, COL, None, None),
        P(ROW, COL),
        P(ROW, COL),
        P(ROW, COL),
        P(),
        P(ALL, None),
    )
    out_specs = (P(ALL, None), P())
    return jax.shard_map(body, mesh=fine, in_specs=in_specs, out_specs=out_specs, check_vma=False)
```

```python
import jax
import jax.numpy as jnp
from jax import lax
from jax.sharding import Mesh, PartitionSpec as P

REACH = 4
ROW = ("zlo", "x")
COL = ("zhi", "y", "core")
ALL = ROW + COL


def from_behind(value, steps):
    count = lax.axis_size(COL)
    pairs = [(source, (source + steps) % count) for source in range(count)]
    return lax.ppermute(value, COL, pairs)


def exchange_sum(part, axes):
    peers = lax.axis_size(axes)
    pieces = part.reshape(peers, part.shape[0] // peers, part.shape[1])
    pieces = lax.all_to_all(pieces, axes, 0, 0, tiled=True)
    return pieces.sum(axis=0)


def exchange_gather(part, axes):
    peers = lax.axis_size(axes)
    copies = jnp.broadcast_to(part[None], (peers,) + part.shape)
    copies = lax.all_to_all(copies, axes, 0, 0, tiled=True)
    return copies.reshape(peers * part.shape[0], *part.shape[1:])


def reduce_all(stacked, scale):
    part = exchange_sum(stacked, "core")
    part = exchange_sum(part, ROW)
    part = exchange_sum(part, ("zhi", "y"))
    part = (part * scale).astype(jnp.bfloat16)
    part = exchange_gather(part, ("zhi", "y"))
    part = exchange_gather(part, ROW)
    return exchange_gather(part, "core").astype(jnp.float32)


def gather_row(features):
    return exchange_gather(features, ROW)


def body(features, adj_tiles, tile_rows, tile_cols, tile_count, weight, cotangent):
    width = features.shape[1]
    own_nodes = features.shape[0]
    tile_size = adj_tiles.shape[2]
    row_count = lax.axis_size(ROW)
    col_count = lax.axis_size(COL)
    tiles = adj_tiles[0]
    slots = tiles.shape[0]
    cols = tile_cols[0]
    live = jnp.arange(slots) < tile_count[0, 0]
    offsets = (tile_rows[0] - lax.axis_index(COL)) % col_count
    w_self = weight[:width]
    w_neigh = weight[width:]

    col_feats = gather_row(features)
    chosen = jnp.take(col_feats.reshape(row_count, tile_size, width), cols, axis=0)
    projected = jnp.dot(chosen.reshape(slots * tile_size, width), w_neigh,
                        preferred_element_type=jnp.float32).astype(jnp.bfloat16)
    placing = (offsets[None, :] == jnp.arange(REACH)[:, None]) & live[None, :]
    placed = jnp.where(placing[:, :, None, None], tiles[None], jnp.zeros_like(tiles[None]))
    placed = placed.transpose(0, 2, 1, 3).reshape(REACH * tile_size, slots * tile_size)
    stacked_sums = jnp.dot(placed, projected, preferred_element_type=jnp.float32)
    stacked_sums = stacked_sums.reshape(REACH, tile_size, width)
    first = from_behind(jnp.stack([stacked_sums[1], stacked_sums[3]]), 1)
    second = from_behind(first[1] + stacked_sums[2], 2)
    neighbour = stacked_sums[0] + first[0] + second

    pre_act = jnp.dot(features, w_self, preferred_element_type=jnp.float32) + neighbour
    hidden = jax.nn.silu(pre_act).astype(jnp.bfloat16)
    sigmoid_z = jax.nn.sigmoid(pre_act)
    slope = sigmoid_z * (1.0 + pre_act * (1.0 - sigmoid_z))
    upstream = (cotangent.astype(jnp.float32) * slope).astype(jnp.bfloat16)
    grad_self = jnp.dot(features.T, upstream, preferred_element_type=jnp.float32)

    window = [upstream] + [from_behind(upstream, -step) for step in range(1, REACH)]
    window = jnp.stack(window)
    reached = jnp.take(window, offsets, axis=0).reshape(slots * tile_size, width)
    mixed = jnp.einsum("tij,tjx->tix", tiles, chosen, preferred_element_type=jnp.float32)
    mixed = jnp.where(live[:, None, None], mixed, 0.0).reshape(slots * tile_size, width)
    high = mixed.astype(jnp.bfloat16)
    low = (mixed - high.astype(jnp.float32)).astype(jnp.bfloat16)
    grad_neigh = jnp.dot(high.T, reached, preferred_element_type=jnp.float32)
    grad_neigh = grad_neigh + jnp.dot(low.T, reached, preferred_element_type=jnp.float32)

    stacked = jnp.concatenate([grad_self, grad_neigh], axis=0)
    total_nodes = own_nodes * row_count * col_count
    weight_grad = reduce_all(stacked, float(total_nodes) ** (-0.5))
    return (hidden, weight_grad)


def solution(mesh):
    rows, cols = mesh.devices.shape
    fine = Mesh(mesh.devices.reshape(2, rows // 2, 4, cols // 8, 2), ALL)
    in_specs = (
        P(ALL, None),
        P(ROW, COL, None, None),
        P(ROW, COL),
        P(ROW, COL),
        P(ROW, COL),
        P(),
        P(ALL, None),
    )
    out_specs = (P(ALL, None), P())
    return jax.shard_map(body, mesh=fine, in_specs=in_specs, out_specs=out_specs, check_vma=False)
```

```python
import jax
import jax.numpy as jnp
from jax import lax
from jax.sharding import Mesh, PartitionSpec as P

REACH = 4
ROW = ("zlo", "x")
COL = ("zhi", "y", "core")
ALL = ROW + COL


def from_behind(value, steps):
    count = lax.axis_size(COL)
    pairs = [(source, (source + steps) % count) for source in range(count)]
    return lax.ppermute(value, COL, pairs)


def exchange_sum(part, axes):
    peers = lax.axis_size(axes)
    pieces = part.reshape(peers, part.shape[0] // peers, part.shape[1])
    pieces = lax.all_to_all(pieces, axes, 0, 0, tiled=True)
    return pieces.sum(axis=0)


def exchange_gather(part, axes):
    peers = lax.axis_size(axes)
    copies = jnp.broadcast_to(part[None], (peers,) + part.shape)
    copies = lax.all_to_all(copies, axes, 0, 0, tiled=True)
    return copies.reshape(peers * part.shape[0], *part.shape[1:])


def reduce_all(stacked, scale):
    part = exchange_sum(stacked, "core")
    part = exchange_sum(part, ("zhi", "y"))
    part = exchange_sum(part, ROW)
    part = (part * scale).astype(jnp.bfloat16)
    part = exchange_gather(part, ROW)
    part = exchange_gather(part, ("zhi", "y"))
    return exchange_gather(part, "core").astype(jnp.float32)


def gather_row(features):
    return exchange_gather(features, ROW)


def body(features, adj_tiles, tile_rows, tile_cols, tile_count, weight, cotangent):
    width = features.shape[1]
    own_nodes = features.shape[0]
    tile_size = adj_tiles.shape[2]
    row_count = lax.axis_size(ROW)
    col_count = lax.axis_size(COL)
    tiles = adj_tiles[0]
    slots = tiles.shape[0]
    cols = tile_cols[0]
    live = jnp.arange(slots) < tile_count[0, 0]
    offsets = (tile_rows[0] - lax.axis_index(COL)) % col_count
    w_self = weight[:width]
    w_neigh = weight[width:]

    col_feats = gather_row(features)
    chosen = jnp.take(col_feats.reshape(row_count, tile_size, width), cols, axis=0)
    projected = jnp.dot(chosen.reshape(slots * tile_size, width), w_neigh,
                        preferred_element_type=jnp.float32).astype(jnp.bfloat16)
    placing = (offsets[None, :] == jnp.arange(REACH)[:, None]) & live[None, :]
    placed = jnp.where(placing[:, :, None, None], tiles[None], jnp.zeros_like(tiles[None]))
    placed = placed.transpose(0, 2, 1, 3).reshape(REACH * tile_size, slots * tile_size)
    stacked_sums = jnp.dot(placed, projected, preferred_element_type=jnp.float32)
    stacked_sums = stacked_sums.reshape(REACH, tile_size, width)
    first = from_behind(jnp.stack([stacked_sums[1], stacked_sums[3]]), 1)
    second = from_behind(first[1] + stacked_sums[2], 2)
    neighbour = stacked_sums[0] + first[0] + second

    pre_act = jnp.dot(features, w_self, preferred_element_type=jnp.float32) + neighbour
    hidden = jax.nn.silu(pre_act).astype(jnp.bfloat16)
    sigmoid_z = jax.nn.sigmoid(pre_act)
    slope = sigmoid_z * (1.0 + pre_act * (1.0 - sigmoid_z))
    upstream = (cotangent.astype(jnp.float32) * slope).astype(jnp.bfloat16)
    grad_self = jnp.dot(features.T, upstream, preferred_element_type=jnp.float32)

    window = [upstream] + [from_behind(upstream, -step) for step in range(1, REACH)]
    window = jnp.stack(window)
    reached = jnp.take(window, offsets, axis=0).reshape(slots * tile_size, width)
    mixed = jnp.einsum("tij,tjx->tix", tiles, chosen, preferred_element_type=jnp.float32)
    mixed = jnp.where(live[:, None, None], mixed, 0.0).reshape(slots * tile_size, width)
    high = mixed.astype(jnp.bfloat16)
    low = (mixed - high.astype(jnp.float32)).astype(jnp.bfloat16)
    grad_neigh = jnp.dot(high.T, reached, preferred_element_type=jnp.float32)
    grad_neigh = grad_neigh + jnp.dot(low.T, reached, preferred_element_type=jnp.float32)

    stacked = jnp.concatenate([grad_self, grad_neigh], axis=0)
    total_nodes = own_nodes * row_count * col_count
    weight_grad = reduce_all(stacked, float(total_nodes) ** (-0.5))
    return (hidden, weight_grad)


def solution(mesh):
    rows, cols = mesh.devices.shape
    fine = Mesh(mesh.devices.reshape(2, rows // 2, 4, cols // 8, 2), ALL)
    in_specs = (
        P(ALL, None),
        P(ROW, COL, None, None),
        P(ROW, COL),
        P(ROW, COL),
        P(ROW, COL),
        P(),
        P(ALL, None),
    )
    out_specs = (P(ALL, None), P())
    return jax.shard_map(body, mesh=fine, in_specs=in_specs, out_specs=out_specs, check_vma=False)
```

```python
import jax
import jax.numpy as jnp
from jax import lax
from jax.sharding import Mesh, PartitionSpec as P

REACH = 4
ROW = ("zlo", "x")
COL = ("zhi", "y", "core")
ALL = ROW + COL


def from_behind(value, steps):
    count = lax.axis_size(COL)
    pairs = [(source, (source + steps) % count) for source in range(count)]
    return lax.ppermute(value, COL, pairs)


def exchange_sum(part, axes):
    peers = lax.axis_size(axes)
    pieces = part.reshape(peers, part.shape[0] // peers, part.shape[1])
    pieces = lax.all_to_all(pieces, axes, 0, 0, tiled=True)
    return pieces.sum(axis=0)


def exchange_gather(part, axes):
    peers = lax.axis_size(axes)
    copies = jnp.broadcast_to(part[None], (peers,) + part.shape)
    copies = lax.all_to_all(copies, axes, 0, 0, tiled=True)
    return copies.reshape(peers * part.shape[0], *part.shape[1:])


def reduce_all(stacked, scale):
    part = exchange_sum(stacked, "core")
    part = exchange_sum(part, ROW)
    part = exchange_sum(part, ("zhi", "y"))
    part = (part * scale).astype(jnp.bfloat16)
    part = exchange_gather(part, ("zhi", "y"))
    part = exchange_gather(part, ROW)
    return exchange_gather(part, "core").astype(jnp.float32)


def gather_row(features):
    return exchange_gather(features, ROW)


def body(features, adj_tiles, tile_rows, tile_cols, tile_count, weight, cotangent):
    width = features.shape[1]
    own_nodes = features.shape[0]
    tile_size = adj_tiles.shape[2]
    row_count = lax.axis_size(ROW)
    col_count = lax.axis_size(COL)
    tiles = adj_tiles[0]
    slots = tiles.shape[0]
    cols = tile_cols[0]
    live = jnp.arange(slots) < tile_count[0, 0]
    offsets = (tile_rows[0] - lax.axis_index(COL)) % col_count
    w_self = weight[:width]
    w_neigh = weight[width:]

    col_feats = gather_row(features)
    chosen = jnp.take(col_feats.reshape(row_count, tile_size, width), cols, axis=0)
    projected = jnp.dot(chosen.reshape(slots * tile_size, width), w_neigh,
                        preferred_element_type=jnp.float32).astype(jnp.bfloat16)
    placing = (offsets[None, :] == jnp.arange(REACH)[:, None]) & live[None, :]
    placed = jnp.where(placing[:, :, None, None], tiles[None], jnp.zeros_like(tiles[None]))
    placed = placed.transpose(0, 2, 1, 3).reshape(REACH * tile_size, slots * tile_size)
    stacked_sums = jnp.dot(placed, projected, preferred_element_type=jnp.float32)
    stacked_sums = stacked_sums.reshape(REACH, tile_size, width)
    carry = from_behind(stacked_sums[REACH - 1], 1)
    for step in range(REACH - 2, 0, -1):
        carry = from_behind(carry + stacked_sums[step], 1)
    neighbour = stacked_sums[0] + carry

    pre_act = jnp.dot(features, w_self, preferred_element_type=jnp.float32) + neighbour
    hidden = jax.nn.silu(pre_act).astype(jnp.bfloat16)
    sigmoid_z = jax.nn.sigmoid(pre_act)
    slope = sigmoid_z * (1.0 + pre_act * (1.0 - sigmoid_z))
    upstream = (cotangent.astype(jnp.float32) * slope).astype(jnp.bfloat16)
    grad_self = jnp.dot(features.T, upstream, preferred_element_type=jnp.float32)

    window = [upstream] + [from_behind(upstream, -step) for step in range(1, REACH)]
    window = jnp.stack(window)
    reached = jnp.take(window, offsets, axis=0).reshape(slots * tile_size, width)
    mixed = jnp.einsum("tij,tjx->tix", tiles, chosen, preferred_element_type=jnp.float32)
    mixed = jnp.where(live[:, None, None], mixed, 0.0).reshape(slots * tile_size, width)
    high = mixed.astype(jnp.bfloat16)
    low = (mixed - high.astype(jnp.float32)).astype(jnp.bfloat16)
    grad_neigh = jnp.dot(high.T, reached, preferred_element_type=jnp.float32)
    grad_neigh = grad_neigh + jnp.dot(low.T, reached, preferred_element_type=jnp.float32)

    stacked = jnp.concatenate([grad_self, grad_neigh], axis=0)
    total_nodes = own_nodes * row_count * col_count
    weight_grad = reduce_all(stacked, float(total_nodes) ** (-0.5))
    return (hidden, weight_grad)


def solution(mesh):
    rows, cols = mesh.devices.shape
    fine = Mesh(mesh.devices.reshape(2, rows // 2, 4, cols // 8, 2), ALL)
    in_specs = (
        P(ALL, None),
        P(ROW, COL, None, None),
        P(ROW, COL),
        P(ROW, COL),
        P(ROW, COL),
        P(),
        P(ALL, None),
    )
    out_specs = (P(ALL, None), P())
    return jax.shard_map(body, mesh=fine, in_specs=in_specs, out_specs=out_specs, check_vma=False)
```

```python
import jax
import jax.numpy as jnp
from jax import lax
from jax.sharding import Mesh, PartitionSpec as P

REACH = 4
ROW = ("zlo", "x")
COL = ("zhi", "y", "core")
ALL = ROW + COL


def from_behind(value, steps):
    count = lax.axis_size(COL)
    pairs = [(source, (source + steps) % count) for source in range(count)]
    return lax.ppermute(value, COL, pairs)


def exchange_sum(part, axes):
    peers = lax.axis_size(axes)
    pieces = part.reshape(peers, part.shape[0] // peers, part.shape[1])
    pieces = lax.all_to_all(pieces, axes, 0, 0, tiled=True)
    return pieces.sum(axis=0)


def exchange_gather(part, axes):
    peers = lax.axis_size(axes)
    copies = jnp.broadcast_to(part[None], (peers,) + part.shape)
    copies = lax.all_to_all(copies, axes, 0, 0, tiled=True)
    return copies.reshape(peers * part.shape[0], *part.shape[1:])


def reduce_all(stacked, scale):
    part = exchange_sum(stacked, "core")
    part = exchange_sum(part, ROW)
    part = exchange_sum(part, ("zhi", "y"))
    part = (part * scale).astype(jnp.bfloat16)
    part = exchange_gather(part, ("zhi", "y"))
    part = exchange_gather(part, ROW)
    return exchange_gather(part, "core").astype(jnp.float32)


def gather_row(features):
    return exchange_gather(features, ROW)


def body(features, adj_tiles, tile_rows, tile_cols, tile_count, weight, cotangent):
    width = features.shape[1]
    own_nodes = features.shape[0]
    tile_size = adj_tiles.shape[2]
    row_count = lax.axis_size(ROW)
    col_count = lax.axis_size(COL)
    tiles = adj_tiles[0]
    slots = tiles.shape[0]
    cols = tile_cols[0]
    live = jnp.arange(slots) < tile_count[0, 0]
    offsets = (tile_rows[0] - lax.axis_index(COL)) % col_count
    w_self = weight[:width]
    w_neigh = weight[width:]

    col_feats = gather_row(features)
    chosen = jnp.take(col_feats.reshape(row_count, tile_size, width), cols, axis=0)
    projected = jnp.dot(chosen.reshape(slots * tile_size, width), w_neigh,
                        preferred_element_type=jnp.float32).astype(jnp.bfloat16)
    placing = (offsets[None, :] == jnp.arange(REACH)[:, None]) & live[None, :]
    placed = jnp.where(placing[:, :, None, None], tiles[None], jnp.zeros_like(tiles[None]))
    placed = placed.transpose(0, 2, 1, 3).reshape(REACH * tile_size, slots * tile_size)
    stacked_sums = jnp.dot(placed, projected, preferred_element_type=jnp.float32)
    stacked_sums = stacked_sums.reshape(REACH, tile_size, width)
    nearest = from_behind(stacked_sums[1], 1)
    carried = from_behind(stacked_sums[3], 1)
    second = from_behind(carried + stacked_sums[2], 2)
    neighbour = stacked_sums[0] + nearest + second

    pre_act = jnp.dot(features, w_self, preferred_element_type=jnp.float32) + neighbour
    hidden = jax.nn.silu(pre_act).astype(jnp.bfloat16)
    sigmoid_z = jax.nn.sigmoid(pre_act)
    slope = sigmoid_z * (1.0 + pre_act * (1.0 - sigmoid_z))
    upstream = (cotangent.astype(jnp.float32) * slope).astype(jnp.bfloat16)
    grad_self = jnp.dot(features.T, upstream, preferred_element_type=jnp.float32)

    window = [upstream] + [from_behind(upstream, -step) for step in range(1, REACH)]
    window = jnp.stack(window)
    reached = jnp.take(window, offsets, axis=0).reshape(slots * tile_size, width)
    mixed = jnp.einsum("tij,tjx->tix", tiles, chosen, preferred_element_type=jnp.float32)
    mixed = jnp.where(live[:, None, None], mixed, 0.0).reshape(slots * tile_size, width)
    high = mixed.astype(jnp.bfloat16)
    low = (mixed - high.astype(jnp.float32)).astype(jnp.bfloat16)
    grad_neigh = jnp.dot(high.T, reached, preferred_element_type=jnp.float32)
    grad_neigh = grad_neigh + jnp.dot(low.T, reached, preferred_element_type=jnp.float32)

    stacked = jnp.concatenate([grad_self, grad_neigh], axis=0)
    total_nodes = own_nodes * row_count * col_count
    weight_grad = reduce_all(stacked, float(total_nodes) ** (-0.5))
    return (hidden, weight_grad)


def solution(mesh):
    rows, cols = mesh.devices.shape
    fine = Mesh(mesh.devices.reshape(2, rows // 2, 4, cols // 8, 2), ALL)
    in_specs = (
        P(ALL, None),
        P(ROW, COL, None, None),
        P(ROW, COL),
        P(ROW, COL),
        P(ROW, COL),
        P(),
        P(ALL, None),
    )
    out_specs = (P(ALL, None), P())
    return jax.shard_map(body, mesh=fine, in_specs=in_specs, out_specs=out_specs, check_vma=False)
```

```python
import jax
import jax.numpy as jnp
from jax import lax
from jax.sharding import Mesh, PartitionSpec as P

REACH = 4
ROW = ("zlo", "x")
COL = ("zhi", "y", "core")
ALL = ROW + COL


def from_behind(value, steps):
    count = lax.axis_size(COL)
    pairs = [(source, (source + steps) % count) for source in range(count)]
    return lax.ppermute(value, COL, pairs)


def exchange_sum(part, axes):
    peers = lax.axis_size(axes)
    pieces = part.reshape(peers, part.shape[0] // peers, part.shape[1])
    pieces = lax.all_to_all(pieces, axes, 0, 0, tiled=True)
    return pieces.sum(axis=0)


def exchange_gather(part, axes):
    peers = lax.axis_size(axes)
    copies = jnp.broadcast_to(part[None], (peers,) + part.shape)
    copies = lax.all_to_all(copies, axes, 0, 0, tiled=True)
    return copies.reshape(peers * part.shape[0], *part.shape[1:])


def swap_core(value):
    return lax.ppermute(value, "core", [(0, 1), (1, 0)])


def reduce_all(stacked, scale):
    first = lax.axis_index("core") == 0
    halves = stacked.reshape(2, stacked.shape[0] // 2, stacked.shape[1])
    kept = jnp.where(first, halves[0], halves[1])
    part = kept + swap_core(jnp.where(first, halves[1], halves[0]))
    part = exchange_sum(part, ROW)
    part = exchange_sum(part, ("zhi", "y"))
    part = (part * scale).astype(jnp.bfloat16)
    part = exchange_gather(part, ("zhi", "y"))
    part = exchange_gather(part, ROW)
    other = swap_core(part)
    whole = jnp.where(first, jnp.concatenate([part, other]), jnp.concatenate([other, part]))
    return whole.astype(jnp.float32)


def gather_row(features):
    return exchange_gather(features, ROW)


def body(features, adj_tiles, tile_rows, tile_cols, tile_count, weight, cotangent):
    width = features.shape[1]
    own_nodes = features.shape[0]
    tile_size = adj_tiles.shape[2]
    row_count = lax.axis_size(ROW)
    col_count = lax.axis_size(COL)
    tiles = adj_tiles[0]
    slots = tiles.shape[0]
    cols = tile_cols[0]
    live = jnp.arange(slots) < tile_count[0, 0]
    offsets = (tile_rows[0] - lax.axis_index(COL)) % col_count
    w_self = weight[:width]
    w_neigh = weight[width:]

    col_feats = gather_row(features)
    chosen = jnp.take(col_feats.reshape(row_count, tile_size, width), cols, axis=0)
    projected = jnp.dot(chosen.reshape(slots * tile_size, width), w_neigh,
                        preferred_element_type=jnp.float32).astype(jnp.bfloat16)
    placing = (offsets[None, :] == jnp.arange(REACH)[:, None]) & live[None, :]
    placed = jnp.where(placing[:, :, None, None], tiles[None], jnp.zeros_like(tiles[None]))
    placed = placed.transpose(0, 2, 1, 3).reshape(REACH * tile_size, slots * tile_size)
    stacked_sums = jnp.dot(placed, projected, preferred_element_type=jnp.float32)
    stacked_sums = stacked_sums.reshape(REACH, tile_size, width)
    first = from_behind(jnp.stack([stacked_sums[1], stacked_sums[3]]), 1)
    second = from_behind(first[1] + stacked_sums[2], 2)
    neighbour = stacked_sums[0] + first[0] + second

    pre_act = jnp.dot(features, w_self, preferred_element_type=jnp.float32) + neighbour
    hidden = jax.nn.silu(pre_act).astype(jnp.bfloat16)
    sigmoid_z = jax.nn.sigmoid(pre_act)
    slope = sigmoid_z * (1.0 + pre_act * (1.0 - sigmoid_z))
    upstream = (cotangent.astype(jnp.float32) * slope).astype(jnp.bfloat16)
    grad_self = jnp.dot(features.T, upstream, preferred_element_type=jnp.float32)

    window = [upstream] + [from_behind(upstream, -step) for step in range(1, REACH)]
    window = jnp.stack(window)
    reached = jnp.take(window, offsets, axis=0).reshape(slots * tile_size, width)
    mixed = jnp.einsum("tij,tjx->tix", tiles, chosen, preferred_element_type=jnp.float32)
    mixed = jnp.where(live[:, None, None], mixed, 0.0).reshape(slots * tile_size, width)
    high = mixed.astype(jnp.bfloat16)
    low = (mixed - high.astype(jnp.float32)).astype(jnp.bfloat16)
    grad_neigh = jnp.dot(high.T, reached, preferred_element_type=jnp.float32)
    grad_neigh = grad_neigh + jnp.dot(low.T, reached, preferred_element_type=jnp.float32)

    stacked = jnp.concatenate([grad_self, grad_neigh], axis=0)
    total_nodes = own_nodes * row_count * col_count
    weight_grad = reduce_all(stacked, float(total_nodes) ** (-0.5))
    return (hidden, weight_grad)


def solution(mesh):
    rows, cols = mesh.devices.shape
    fine = Mesh(mesh.devices.reshape(2, rows // 2, 4, cols // 8, 2), ALL)
    in_specs = (
        P(ALL, None),
        P(ROW, COL, None, None),
        P(ROW, COL),
        P(ROW, COL),
        P(ROW, COL),
        P(),
        P(ALL, None),
    )
    out_specs = (P(ALL, None), P())
    return jax.shard_map(body, mesh=fine, in_specs=in_specs, out_specs=out_specs, check_vma=False)
```

```python
import jax
import jax.numpy as jnp
from jax import lax
from jax.sharding import Mesh, PartitionSpec as P

REACH = 4
ROW = ("zlo", "x")
COL = ("zhi", "y", "core")
ALL = ROW + COL


def from_behind(value, steps):
    count = lax.axis_size(COL)
    pairs = [(source, (source + steps) % count) for source in range(count)]
    return lax.ppermute(value, COL, pairs)


def exchange_sum(part, axes):
    peers = lax.axis_size(axes)
    pieces = part.reshape(peers, part.shape[0] // peers, part.shape[1])
    pieces = lax.all_to_all(pieces, axes, 0, 0, tiled=True)
    return pieces.sum(axis=0)


def exchange_gather(part, axes):
    peers = lax.axis_size(axes)
    copies = jnp.broadcast_to(part[None], (peers,) + part.shape)
    copies = lax.all_to_all(copies, axes, 0, 0, tiled=True)
    return copies.reshape(peers * part.shape[0], *part.shape[1:])


def reduce_all(stacked, scale):
    part = exchange_sum(stacked, "core")
    part = exchange_sum(part, ROW)
    part = exchange_sum(part, ("zhi", "y"))
    part = (part * scale).astype(jnp.bfloat16)
    part = exchange_gather(part, ("zhi", "y"))
    part = exchange_gather(part, ROW)
    return exchange_gather(part, "core").astype(jnp.float32)


def gather_row(features):
    return exchange_gather(features, ROW)


def body(features, adj_tiles, tile_rows, tile_cols, tile_count, weight, cotangent):
    width = features.shape[1]
    own_nodes = features.shape[0]
    tile_size = adj_tiles.shape[2]
    row_count = lax.axis_size(ROW)
    col_count = lax.axis_size(COL)
    tiles = adj_tiles[0]
    slots = tiles.shape[0]
    cols = tile_cols[0]
    live = jnp.arange(slots) < tile_count[0, 0]
    offsets = (tile_rows[0] - lax.axis_index(COL)) % col_count
    w_self = weight[:width]
    w_neigh = weight[width:]

    col_feats = gather_row(features)
    chosen = jnp.take(col_feats.reshape(row_count, tile_size, width), cols, axis=0)
    projected = jnp.dot(chosen.reshape(slots * tile_size, width), w_neigh,
                        preferred_element_type=jnp.float32).astype(jnp.bfloat16)
    placing = (offsets[None, :] == jnp.arange(REACH)[:, None]) & live[None, :]
    placed = jnp.where(placing[:, :, None, None], tiles[None], jnp.zeros_like(tiles[None]))
    placed = placed.transpose(0, 2, 1, 3).reshape(REACH * tile_size, slots * tile_size)
    stacked_sums = jnp.dot(placed, projected, preferred_element_type=jnp.float32)
    stacked_sums = stacked_sums.reshape(REACH, tile_size, width)
    first = from_behind(jnp.stack([stacked_sums[1], stacked_sums[3]]), 1)
    second = from_behind(first[1] + stacked_sums[2], 2)
    neighbour = stacked_sums[0] + first[0] + second

    pre_act = jnp.dot(features, w_self, preferred_element_type=jnp.float32) + neighbour
    hidden = jax.nn.silu(pre_act).astype(jnp.bfloat16)
    sigmoid_z = jax.nn.sigmoid(pre_act)
    slope = sigmoid_z * (1.0 + pre_act * (1.0 - sigmoid_z))
    upstream = (cotangent.astype(jnp.float32) * slope).astype(jnp.bfloat16)
    grad_self = jnp.dot(features.T, upstream, preferred_element_type=jnp.float32)

    ahead = from_behind(upstream, -1)
    farther = from_behind(jnp.stack([upstream, ahead]), -2)
    window = jnp.stack([upstream, ahead, farther[0], farther[1]])
    reached = jnp.take(window, offsets, axis=0).reshape(slots * tile_size, width)
    mixed = jnp.einsum("tij,tjx->tix", tiles, chosen, preferred_element_type=jnp.float32)
    mixed = jnp.where(live[:, None, None], mixed, 0.0).reshape(slots * tile_size, width)
    high = mixed.astype(jnp.bfloat16)
    low = (mixed - high.astype(jnp.float32)).astype(jnp.bfloat16)
    grad_neigh = jnp.dot(high.T, reached, preferred_element_type=jnp.float32)
    grad_neigh = grad_neigh + jnp.dot(low.T, reached, preferred_element_type=jnp.float32)

    stacked = jnp.concatenate([grad_self, grad_neigh], axis=0)
    total_nodes = own_nodes * row_count * col_count
    weight_grad = reduce_all(stacked, float(total_nodes) ** (-0.5))
    return (hidden, weight_grad)


def solution(mesh):
    rows, cols = mesh.devices.shape
    fine = Mesh(mesh.devices.reshape(2, rows // 2, 4, cols // 8, 2), ALL)
    in_specs = (
        P(ALL, None),
        P(ROW, COL, None, None),
        P(ROW, COL),
        P(ROW, COL),
        P(ROW, COL),
        P(),
        P(ALL, None),
    )
    out_specs = (P(ALL, None), P())
    return jax.shard_map(body, mesh=fine, in_specs=in_specs, out_specs=out_specs, check_vma=False)
```
